32 devices in a mesh: batch: 8 (over z, x), phase: 2 (over core), mp: 2 (over y).
Axes of the slice: x: 2, y: 2, z: 4, core: 2. Of those that a mesh axis runs over, the one named last changes fastest.
Arguments:
- images: bfloat16 [64, 4, 4, 768], P('batch'), may hold values from -6 to 6
- conv_kernels: float32 [2, 7, 7, 768], P('phase'), may hold values from -0.875 to 0.875
- norm_gains: float32 [2, 768], P('phase'), may hold values from 0.1 to 1.9
- expand_weight: bfloat16 [2, 768, 3072], P('phase', None, 'mp'), may hold values from -0.21875 to 0.21875
- project_weight: bfloat16 [2, 3072, 768], P('phase', 'mp'), may hold values from -0.109375 to 0.109375
- head_weight: bfloat16 [768, 1024], replicated, may hold values from -0.21875 to 0.21875
- texts: bfloat16 [64, 1024], P('batch'), may hold values from -6 to 6
- pair_index: int32 [64], P('batch'), may hold values from 0 to 63
Outputs:
- input_grads: float32 [2, 64, 4, 4, 768], P('phase', 'batch')
The draws below stay inside these ranges and needn't reach their ends.
Inputs may be any that keep to these rules, and one draw needn't show every extreme that they name: Image i and text pair_index[i] form a positive pair.
All inputs are finite; a program needn't handle non-finite values.
Results may differ from the reference program's by a relative error of at most 0.018.
Values may be sent and summed in bfloat16 or wider, within the bound.
No kernel may reach another device: no remote copies, remote signals or barrier semaphores. Data moves between devices by JAX's collectives and lax.ppermute only.
A program may use at most 64 MiB of HBM per device.

```python
import jax
import jax.numpy as jnp
import numpy as np
from jax import lax

W = 768
HID = 3072
E = 1024
KSIZE = 7
SIDE = 4
IMAGES = 64
TEXTS = 64
N_PHASE = 2


def place_ends(array, key, smallest, largest):
    longest = array.shape.index(max(array.shape))
    spots = []
    for shift in (0, 1):
        where = [jax.random.randint(jax.random.fold_in(key, axis), (), 0, length) for axis, length in enumerate(array.shape)]
        where[longest] = (where[longest] + shift) % array.shape[longest]
        spots.append(tuple(where))
    return array.at[spots[0]].set(smallest).at[spots[1]].set(largest)


def level_of(key, dims, pieces, smallest, largest):
    def one(position, parts):
        draws = jax.random.uniform(jax.random.fold_in(jax.random.fold_in(key, 6), position), (parts,), jnp.float32, smallest / len(pieces), largest / len(pieces))
        return jnp.repeat(jnp.exp(draws), dims[position] // parts).reshape((-1,) + (1,) * (len(dims) - position - 1))

    loudness = one(*pieces[0])
    for cut in pieces[1:]:
        loudness = loudness * one(*cut)
    return loudness


def gaussian(stream_key, dims, width, most, shards=(), kind=jnp.bfloat16):
    entries = width * jax.random.normal(stream_key, dims, jnp.float32)
    if shards:
        entries = entries * level_of(stream_key, dims, shards, -0.22, 0.18)
    return jnp.clip(entries, -most, most).astype(kind)


def setup_inputs(seed: int = 0) -> dict:
    splits = jax.random.split(jax.random.key(seed), 9)
    return {
        "images": gaussian(splits[0], (IMAGES, SIDE, SIDE, W), 1.0, 6.0, ((0, 8),)),
        "conv_kernels": gaussian(splits[1], (N_PHASE, KSIZE, KSIZE, W), (KSIZE * KSIZE) ** -0.5, 0.875, ((0, 2),), jnp.float32),
        "norm_gains": jnp.clip(1.0 + 0.18 * jax.random.normal(splits[2], (N_PHASE, W), jnp.float32), 0.1, 1.9),
        "expand_weight": gaussian(splits[3], (N_PHASE, W, HID), W ** -0.5, 0.21875, ((0, 2), (2, 2))),
        "project_weight": gaussian(splits[4], (N_PHASE, HID, W), HID ** -0.5, 0.109375, ((0, 2), (1, 2))),
        "head_weight": gaussian(splits[5], (W, E), W ** -0.5, 0.21875),
        "texts": gaussian(splits[6], (TEXTS, E), 1.0, 6.0, ((0, 8),)),
        "pair_index": place_ends(jax.random.randint(splits[7], (IMAGES,), 0, TEXTS), jax.random.fold_in(splits[7], 1), 0, TEXTS - 1).astype(jnp.int32),
    }


inverse_softness_factor = 30.0

def depthwise(values, kernel):
    kernel_side = kernel.shape[0]
    margin = kernel_side // 2
    grid_side = values.shape[1]
    cells = np.arange(grid_side * grid_side)
    cell_row = cells // grid_side
    cell_col = cells % grid_side
    tap_row = np.clip(cell_row[None, :] - cell_row[:, None] + margin, 0, kernel_side - 1)
    tap_col = np.clip(cell_col[None, :] - cell_col[:, None] + margin, 0, kernel_side - 1)
    inside = ((np.abs(cell_row[None, :] - cell_row[:, None]) <= margin) & (np.abs(cell_col[None, :] - cell_col[:, None]) <= margin)).astype(np.float32)
    operator = kernel[tap_row, tap_col] * jnp.asarray(inside, dtype=kernel.dtype)[:, :, None]
    flat = values.reshape(values.shape[0], grid_side * grid_side, values.shape[3])
    result = jnp.einsum('oic,bic->boc', operator, flat, precision=lax.Precision.HIGHEST)
    return result.reshape(values.shape)

def normalize_last(values):
    centred = values - lax.optimization_barrier(jnp.mean(values, axis=-1, keepdims=True))
    variance = lax.optimization_barrier(jnp.mean(centred * centred, axis=-1, keepdims=True))
    return centred * lax.rsqrt(variance + 1e-06)

def front_part(values, kernel, gain_vec):
    return normalize_last(depthwise(values, kernel)) * gain_vec

def mlp_part(normed, expand, project_out):
    flattened = normed.reshape(-1, normed.shape[-1]).astype(jnp.bfloat16)
    hidden = jax.nn.gelu(jnp.dot(flattened, expand, preferred_element_type=jnp.float32)).astype(jnp.bfloat16)
    return jnp.dot(hidden, project_out, preferred_element_type=jnp.float32).reshape(normed.shape)

def head_part(values, head_weight):
    pooled = lax.optimization_barrier(jnp.mean(values, axis=(1, 2)))
    normed = normalize_last(pooled).astype(jnp.bfloat16)
    embedded = jnp.dot(normed, head_weight, preferred_element_type=jnp.float32)
    return embedded * lax.rsqrt(lax.optimization_barrier(jnp.sum(embedded * embedded, axis=-1, keepdims=True)) + 1e-06)

def unit_text(texts):
    widened = texts.astype(jnp.float32)
    return (widened * lax.rsqrt(lax.optimization_barrier(jnp.sum(widened * widened, axis=-1, keepdims=True)) + 1e-06)).astype(jnp.bfloat16)

def reference(images, conv_kernels, norm_gains, expand_weight, project_weight, head_weight, texts, pair_index):

    def forward(inputs_low, section):
        widened = inputs_low.astype(jnp.float32)
        normed, front_back = jax.vjp(lambda inner: front_part(inner, conv_kernels[section], norm_gains[section]), widened)
        branch, mlp_back = jax.vjp(lambda inner: mlp_part(inner, expand_weight[section], project_weight[section]), normed)
        return ((widened + branch).astype(jnp.bfloat16), front_back, mlp_back)

    def backward(cotangent, front_back, mlp_back):
        partial_grad, = mlp_back(cotangent)
        from_front, = front_back(partial_grad)
        return cotangent + from_front
    first_out, front_one, mlp_one = forward(images, 0)
    second_out, front_two, mlp_two = forward(first_out, 1)
    embed, head_back = jax.vjp(lambda inner: head_part(inner, head_weight), second_out.astype(jnp.float32))
    vector_lowered_total = embed.astype(jnp.bfloat16)
    caption_unit_vectors = unit_text(texts)
    cosine_score_matrix = inverse_softness_factor * jnp.dot(vector_lowered_total, caption_unit_vectors.T, preferred_element_type=jnp.float32)
    weights = jnp.exp(cosine_score_matrix).astype(jnp.bfloat16)
    softmax_denominators = lax.optimization_barrier(jnp.sum(weights.astype(jnp.float32), axis=1))
    softmax_scaled_captions = jnp.dot(weights, caption_unit_vectors, preferred_element_type=jnp.float32)
    diagonal_matched_scores = caption_unit_vectors[pair_index].astype(jnp.float32)
    encoder_output_slope = inverse_softness_factor * (softmax_scaled_captions / softmax_denominators[:, None] - diagonal_matched_scores)
    grad_second, = head_back(encoder_output_slope)
    grad_first_in = backward(grad_second, front_two, mlp_two)
    returned = lax.optimization_barrier(grad_first_in.astype(jnp.bfloat16)).astype(jnp.float32)
    grad_images = backward(returned, front_one, mlp_one)
    return jnp.stack([grad_images, grad_first_in])
```

```python
import jax
import jax.numpy as jnp
import numpy as np
from jax import lax
from jax.sharding import PartitionSpec as P

inverse_softness_factor = 30.0


def swapped(value, axis, stride):
    return lax.ppermute(value, axis, [(i, i ^ 1 << stride) for i in range(lax.axis_size(axis))])


def depthwise(values, kernel):
    kernel_side = kernel.shape[0]
    margin = kernel_side // 2
    grid_side = values.shape[1]
    cells = np.arange(grid_side * grid_side)
    cell_row = cells // grid_side
    cell_col = cells % grid_side
    tap_row = np.clip(cell_row[None, :] - cell_row[:, None] + margin, 0, kernel_side - 1)
    tap_col = np.clip(cell_col[None, :] - cell_col[:, None] + margin, 0, kernel_side - 1)
    inside = (
        (np.abs(cell_row[None, :] - cell_row[:, None]) <= margin)
        & (np.abs(cell_col[None, :] - cell_col[:, None]) <= margin)
    ).astype(np.float32)
    operator = kernel[tap_row, tap_col] * jnp.asarray(inside, dtype=kernel.dtype)[:, :, None]
    flat = values.reshape(values.shape[0], grid_side * grid_side, values.shape[3])
    result = jnp.einsum("oic,bic->boc", operator, flat, precision=lax.Precision.HIGHEST)
    return result.reshape(values.shape)


def normalize_last(values):
    centred = values - jnp.mean(values, axis=-1, keepdims=True)
    variance = jnp.mean(centred * centred, axis=-1, keepdims=True)
    return centred * lax.rsqrt(variance + 1e-06)


def front_part(values, kernel, gain_vec):
    return normalize_last(depthwise(values, kernel)) * gain_vec


def mlp_part(normed, expand, project_out):
    flattened = normed.reshape(-1, normed.shape[-1]).astype(jnp.bfloat16)
    hidden = jax.nn.gelu(jnp.dot(flattened, expand, preferred_element_type=jnp.float32)).astype(
        jnp.bfloat16
    )
    return jnp.dot(hidden, project_out, preferred_element_type=jnp.float32).reshape(normed.shape)


def head_part(values, head_weight):
    pooled = jnp.mean(values, axis=(1, 2))
    normed = normalize_last(pooled).astype(jnp.bfloat16)
    embedded = jnp.dot(normed, head_weight, preferred_element_type=jnp.float32)
    return embedded * lax.rsqrt(jnp.sum(embedded * embedded, axis=-1, keepdims=True) + 1e-06)


def unit_text(texts):
    widened = texts.astype(jnp.float32)
    return (widened * lax.rsqrt(jnp.sum(widened * widened, axis=-1, keepdims=True) + 1e-06)).astype(
        jnp.bfloat16
    )


def hidden_total(values):
    low = values.astype(jnp.bfloat16)
    other = swapped(low, "mp", 0)
    return (low.astype(jnp.float32) + other.astype(jnp.float32)).astype(jnp.bfloat16).astype(jnp.float32)


def gather_rows(block, axis):
    count = lax.axis_size(axis)
    place = lax.axis_index(axis)
    stride = 0
    while (1 << stride) < count:
        other = swapped(block, axis, stride)
        upper = (place >> stride) & 1
        block = jnp.where(
            upper == 0,
            jnp.concatenate([block, other], axis=0),
            jnp.concatenate([other, block], axis=0),
        )
        stride += 1
    return block


def hand_over(values):
    return swapped(values, "phase", 0)


def section_forward(inputs_low, kernel, gain_vec, expand, project_out):
    widened = inputs_low.astype(jnp.float32)
    normed, front_back = jax.vjp(lambda inner: front_part(inner, kernel, gain_vec), widened)
    partial_out, mlp_back = jax.vjp(lambda inner: mlp_part(inner, expand, project_out), normed)
    summed = hidden_total(partial_out)
    return ((widened + summed).astype(jnp.bfloat16), front_back, mlp_back)


def section_backward(cotangent, front_back, mlp_back):
    (partial_grad,) = mlp_back(cotangent)
    (from_front,) = front_back(hidden_total(partial_grad))
    return cotangent + from_front


def make_fold(vector_lowered_total, pair_index, row_map):

    def fold_texts(state_now, text_block, first_row):
        block_rows = text_block.shape[0]
        cosine_score_matrix = inverse_softness_factor * jnp.einsum(
            "ie,je->ij", vector_lowered_total, text_block, preferred_element_type=jnp.float32
        )
        weights = jnp.exp(cosine_score_matrix).astype(jnp.bfloat16)
        softmax_denominators = jnp.sum(weights.astype(jnp.float32), axis=1)
        softmax_scaled_captions = jnp.dot(weights, text_block, preferred_element_type=jnp.float32)
        global_rows = row_map(jnp.arange(block_rows, dtype=jnp.int32))
        onehot = (pair_index[:, None] == global_rows[None, :]).astype(jnp.bfloat16)
        diagonal_matched_scores = jnp.dot(onehot, text_block, preferred_element_type=jnp.float32)
        return (softmax_denominators, softmax_scaled_captions, diagonal_matched_scores)

    return fold_texts


def on_device(
    images, conv_kernels, norm_gains, expand_weight, project_weight, head_weight, texts, pair_index
):
    phase_pick = lax.axis_index("phase")
    kernel = conv_kernels[0]
    gain_vec = norm_gains[0]
    expand = expand_weight[0]
    project_out = project_weight[0]
    first_out, front_one, mlp_one = section_forward(images, kernel, gain_vec, expand, project_out)
    handed = hand_over(first_out)
    second_out, front_two, mlp_two = section_forward(handed, kernel, gain_vec, expand, project_out)
    embed, head_back = jax.vjp(
        lambda inner: head_part(inner, head_weight), second_out.astype(jnp.float32)
    )
    vector_lowered_total = embed.astype(jnp.bfloat16)
    caption_unit_vectors = unit_text(texts)
    image_rows = embed.shape[0]
    embed_width = embed.shape[1]
    text_rows = caption_unit_vectors.shape[0]
    share_count = 1
    share_rows = text_rows // share_count

    def share_map(rows_now):
        return rows_now // share_rows * text_rows + rows_now % share_rows

    start_state = (
        jnp.zeros((image_rows,), jnp.float32),
        jnp.zeros((image_rows, embed_width), jnp.float32),
        jnp.zeros((image_rows, embed_width), jnp.float32),
    )
    fold_texts = make_fold(vector_lowered_total, pair_index, share_map)
    softmax_denominators, softmax_scaled_captions, diagonal_matched_scores = fold_texts(
        start_state, gather_rows(caption_unit_vectors, "batch"), jnp.int32(0)
    )
    encoder_output_slope = inverse_softness_factor * (
        softmax_scaled_captions / softmax_denominators[:, None] - diagonal_matched_scores
    )
    (grad_second,) = head_back(encoder_output_slope)
    grad_first_in = section_backward(grad_second, front_two, mlp_two)
    returned = hand_over(grad_first_in.astype(jnp.bfloat16))
    grad_images = section_backward(returned.astype(jnp.float32), front_one, mlp_one)
    chosen = jnp.where(phase_pick == 0, grad_images, grad_first_in)
    return chosen[None]


def solution(mesh):
    return jax.shard_map(
        on_device,
        mesh=mesh,
        in_specs=(
            P("batch", None, None, None),
            P("phase", None, None, None),
            P("phase", None),
            P("phase", None, "mp"),
            P("phase", "mp", None),
            P(),
            P("batch", None),
            P("batch"),
        ),
        out_specs=P("phase", "batch", None, None, None),
        check_vma=False,
    )
```

```python
import jax
import jax.numpy as jnp
import numpy as np
from jax import lax
from jax.sharding import PartitionSpec as P

inverse_softness_factor = 30.0


def swapped(value, axis, stride):
    return lax.ppermute(value, axis, [(i, i ^ 1 << stride) for i in range(lax.axis_size(axis))])


def depthwise(values, kernel, side):
    margin = kernel.shape[0] // 2
    cells = side * side
    outs = []
    for o in range(cells):
        row_o, col_o = divmod(o, side)
        acc = None
        for i in range(cells):
            row_i, col_i = divmod(i, side)
            d_row, d_col = row_i - row_o, col_i - col_o
            if abs(d_row) > margin or abs(d_col) > margin:
                continue
            term = kernel[d_row + margin, d_col + margin][None, :] * values[i]
            acc = term if acc is None else acc + term
        outs.append(acc)
    return jnp.stack(outs)


def normalize_last(values):
    centred = values - jnp.mean(values, axis=-1, keepdims=True)
    variance = jnp.mean(centred * centred, axis=-1, keepdims=True)
    return centred * lax.rsqrt(variance + 1e-06)


def front_part(values, kernel, gain_vec, side):
    return normalize_last(depthwise(values, kernel, side)) * gain_vec


def mlp_part(normed, expand, project_out):
    flattened = normed.reshape(-1, normed.shape[-1]).astype(jnp.bfloat16)
    hidden = jax.nn.gelu(jnp.dot(flattened, expand, preferred_element_type=jnp.float32)).astype(
        jnp.bfloat16
    )
    return jnp.dot(hidden, project_out, preferred_element_type=jnp.float32).reshape(normed.shape)


def head_part(values, head_weight):
    pooled = jnp.mean(values, axis=0)
    normed = normalize_last(pooled).astype(jnp.bfloat16)
    embedded = jnp.dot(normed, head_weight, preferred_element_type=jnp.float32)
    return embedded * lax.rsqrt(jnp.sum(embedded * embedded, axis=-1, keepdims=True) + 1e-06)


def unit_text(texts):
    widened = texts.astype(jnp.float32)
    return (widened * lax.rsqrt(jnp.sum(widened * widened, axis=-1, keepdims=True) + 1e-06)).astype(
        jnp.bfloat16
    )


def hidden_total(values):
    low = values.astype(jnp.bfloat16)
    other = swapped(low, "mp", 0)
    return (low.astype(jnp.float32) + other.astype(jnp.float32)).astype(jnp.bfloat16).astype(jnp.float32)


def gather_rows(block, axis):
    count = lax.axis_size(axis)
    place = lax.axis_index(axis)
    stride = 0
    while (1 << stride) < count:
        other = swapped(block, axis, stride)
        upper = (place >> stride) & 1
        block = jnp.where(
            upper == 0,
            jnp.concatenate([block, other], axis=0),
            jnp.concatenate([other, block], axis=0),
        )
        stride += 1
    return block


def hand_over(values):
    return swapped(values, "phase", 0)


def section_forward(inputs_low, kernel, gain_vec, expand, project_out, side):
    widened = inputs_low.astype(jnp.float32)
    normed, front_back = jax.vjp(lambda inner: front_part(inner, kernel, gain_vec, side), widened)
    partial_out, mlp_back = jax.vjp(lambda inner: mlp_part(inner, expand, project_out), normed)
    summed = hidden_total(partial_out)
    return ((widened + summed).astype(jnp.bfloat16), front_back, mlp_back)


def section_backward(cotangent, front_back, mlp_back):
    (partial_grad,) = mlp_back(cotangent)
    (from_front,) = front_back(hidden_total(partial_grad))
    return cotangent + from_front


def make_fold(vector_lowered_total, pair_index, row_map):

    def fold_texts(state_now, text_block, first_row):
        block_rows = text_block.shape[0]
        cosine_score_matrix = inverse_softness_factor * jnp.einsum(
            "ie,je->ij", vector_lowered_total, text_block, preferred_element_type=jnp.float32
        )
        weights = jnp.exp(cosine_score_matrix).astype(jnp.bfloat16)
        softmax_denominators = jnp.sum(weights.astype(jnp.float32), axis=1)
        softmax_scaled_captions = jnp.dot(weights, text_block, preferred_element_type=jnp.float32)
        global_rows = row_map(jnp.arange(block_rows, dtype=jnp.int32))
        onehot = (pair_index[:, None] == global_rows[None, :]).astype(jnp.bfloat16)
        diagonal_matched_scores = jnp.dot(onehot, text_block, preferred_element_type=jnp.float32)
        return (softmax_denominators, softmax_scaled_captions, diagonal_matched_scores)

    return fold_texts


def on_device(
    images, conv_kernels, norm_gains, expand_weight, project_weight, head_weight, texts, pair_index
):
    phase_pick = lax.axis_index("phase")
    kernel = conv_kernels[0]
    gain_vec = norm_gains[0]
    expand = expand_weight[0]
    project_out = project_weight[0]
    count, side = images.shape[0], images.shape[1]
    width = images.shape[3]
    cell_major = images.reshape(count, side * side, width).transpose(1, 0, 2)
    first_out, front_one, mlp_one = section_forward(cell_major, kernel, gain_vec, expand, project_out, side)
    handed = hand_over(first_out)
    second_out, front_two, mlp_two = section_forward(handed, kernel, gain_vec, expand, project_out, side)
    embed, head_back = jax.vjp(
        lambda inner: head_part(inner, head_weight), second_out.astype(jnp.float32)
    )
    vector_lowered_total = embed.astype(jnp.bfloat16)
    caption_unit_vectors = unit_text(texts)
    image_rows = embed.shape[0]
    embed_width = embed.shape[1]
    text_rows = caption_unit_vectors.shape[0]
    share_count = 1
    share_rows = text_rows // share_count

    def share_map(rows_now):
        return rows_now // share_rows * text_rows + rows_now % share_rows

    start_state = (
        jnp.zeros((image_rows,), jnp.float32),
        jnp.zeros((image_rows, embed_width), jnp.float32),
        jnp.zeros((image_rows, embed_width), jnp.float32),
    )
    fold_texts = make_fold(vector_lowered_total, pair_index, share_map)
    softmax_denominators, softmax_scaled_captions, diagonal_matched_scores = fold_texts(
        start_state, gather_rows(caption_unit_vectors, "batch"), jnp.int32(0)
    )
    encoder_output_slope = inverse_softness_factor * (
        softmax_scaled_captions / softmax_denominators[:, None] - diagonal_matched_scores
    )
    (grad_second,) = head_back(encoder_output_slope)
    grad_first_in = section_backward(grad_second, front_two, mlp_two)
    returned = hand_over(grad_first_in.astype(jnp.bfloat16))
    grad_images = section_backward(returned.astype(jnp.float32), front_one, mlp_one)
    chosen = jnp.where(phase_pick == 0, grad_images, grad_first_in)
    return chosen.transpose(1, 0, 2).reshape(count, side, side, width)[None]


def solution(mesh):
    return jax.shard_map(
        on_device,
        mesh=mesh,
        in_specs=(
            P("batch", None, None, None),
            P("phase", None, None, None),
            P("phase", None),
            P("phase", None, "mp"),
            P("phase", "mp", None),
            P(),
            P("batch", None),
            P("batch"),
        ),
        out_specs=P("phase", "batch", None, None, None),
        check_vma=False,
    )
```

```python
import jax
import jax.numpy as jnp
import numpy as np
from jax import lax
from jax.sharding import PartitionSpec as P

inverse_softness_factor = 30.0


def swapped(value, axis, stride):
    return lax.ppermute(value, axis, [(i, i ^ 1 << stride) for i in range(lax.axis_size(axis))])


def depthwise(values, kernel, side):
    margin = kernel.shape[0] // 2
    cells = side * side
    outs = []
    for o in range(cells):
        row_o, col_o = divmod(o, side)
        acc = None
        for i in range(cells):
            row_i, col_i = divmod(i, side)
            d_row, d_col = row_i - row_o, col_i - col_o
            if abs(d_row) > margin or abs(d_col) > margin:
                continue
            term = kernel[d_row + margin, d_col + margin][None, :] * values[i]
            acc = term if acc is None else acc + term
        outs.append(acc)
    return jnp.stack(outs)


def normalize_last(values):
    centred = values - jnp.mean(values, axis=-1, keepdims=True)
    variance = jnp.mean(centred * centred, axis=-1, keepdims=True)
    return centred * lax.rsqrt(variance + 1e-06)


def front_part(values, kernel, gain_vec, side):
    return normalize_last(depthwise(values, kernel, side)) * gain_vec


def mlp_part(normed, expand, project_out):
    flattened = normed.reshape(-1, normed.shape[-1]).astype(jnp.bfloat16)
    hidden = jax.nn.gelu(jnp.dot(flattened, expand, preferred_element_type=jnp.float32)).astype(
        jnp.bfloat16
    )
    return jnp.dot(hidden, project_out, preferred_element_type=jnp.float32).reshape(normed.shape)


def head_part(values, head_weight):
    pooled = jnp.mean(values, axis=0)
    normed = normalize_last(pooled).astype(jnp.bfloat16)
    embedded = jnp.dot(normed, head_weight, preferred_element_type=jnp.float32)
    return embedded * lax.rsqrt(jnp.sum(embedded * embedded, axis=-1, keepdims=True) + 1e-06)


def unit_text(texts):
    widened = texts.astype(jnp.float32)
    return (widened * lax.rsqrt(jnp.sum(widened * widened, axis=-1, keepdims=True) + 1e-06)).astype(
        jnp.bfloat16
    )


def hidden_total(values):
    low = values.astype(jnp.bfloat16)
    other = swapped(low, "mp", 0)
    return (low.astype(jnp.float32) + other.astype(jnp.float32)).astype(jnp.bfloat16).astype(jnp.float32)


def gather_rows(block, axis):
    count = lax.axis_size(axis)
    stride = 0
    while (1 << stride) < count:
        block = jnp.concatenate([block, swapped(block, axis, stride)], axis=0)
        stride += 1
    return block


def gathered_row_ids(rows, axis):
    place = lax.axis_index(axis)
    spot = jnp.arange(rows * lax.axis_size(axis), dtype=jnp.int32)
    return jnp.bitwise_xor(place, spot // rows) * rows + spot % rows


def hand_over(values):
    return swapped(values, "phase", 0)


def section_forward(inputs_low, kernel, gain_vec, expand, project_out, side):
    widened = inputs_low.astype(jnp.float32)
    normed, front_back = jax.vjp(lambda inner: front_part(inner, kernel, gain_vec, side), widened)
    partial_out, mlp_back = jax.vjp(lambda inner: mlp_part(inner, expand, project_out), normed)
    summed = hidden_total(partial_out)
    return ((widened + summed).astype(jnp.bfloat16), front_back, mlp_back)


def section_backward(cotangent, front_back, mlp_back):
    (partial_grad,) = mlp_back(cotangent)
    (from_front,) = front_back(hidden_total(partial_grad))
    return cotangent + from_front


def make_fold(vector_lowered_total, pair_index, row_map):

    def fold_texts(state_now, text_block, first_row):
        block_rows = text_block.shape[0]
        cosine_score_matrix = inverse_softness_factor * jnp.einsum(
            "ie,je->ij", vector_lowered_total, text_block, preferred_element_type=jnp.float32
        )
        weights = jnp.exp(cosine_score_matrix).astype(jnp.bfloat16)
        softmax_denominators = jnp.sum(weights.astype(jnp.float32), axis=1)
        softmax_scaled_captions = jnp.dot(weights, text_block, preferred_element_type=jnp.float32)
        global_rows = row_map(block_rows)
        onehot = (pair_index[:, None] == global_rows[None, :]).astype(jnp.bfloat16)
        diagonal_matched_scores = jnp.dot(onehot, text_block, preferred_element_type=jnp.float32)
        return (softmax_denominators, softmax_scaled_captions, diagonal_matched_scores)

    return fold_texts


def on_device(
    images, conv_kernels, norm_gains, expand_weight, project_weight, head_weight, texts, pair_index
):
    phase_pick = lax.axis_index("phase")
    kernel = conv_kernels[0]
    gain_vec = norm_gains[0]
    expand = expand_weight[0]
    project_out = project_weight[0]
    count, side = images.shape[0], images.shape[1]
    width = images.shape[3]
    cell_major = images.reshape(count, side * side, width).transpose(1, 0, 2)
    first_out, front_one, mlp_one = section_forward(cell_major, kernel, gain_vec, expand, project_out, side)
    handed = hand_over(first_out)
    second_out, front_two, mlp_two = section_forward(handed, kernel, gain_vec, expand, project_out, side)
    embed, head_back = jax.vjp(
        lambda inner: head_part(inner, head_weight), second_out.astype(jnp.float32)
    )
    vector_lowered_total = embed.astype(jnp.bfloat16)
    caption_unit_vectors = unit_text(texts)
    image_rows = embed.shape[0]
    embed_width = embed.shape[1]
    text_rows = caption_unit_vectors.shape[0]
    share_count = 1
    share_rows = text_rows // share_count

    def share_map(block_rows):
        return gathered_row_ids(text_rows, "batch")

    start_state = (
        jnp.zeros((image_rows,), jnp.float32),
        jnp.zeros((image_rows, embed_width), jnp.float32),
        jnp.zeros((image_rows, embed_width), jnp.float32),
    )
    fold_texts = make_fold(vector_lowered_total, pair_index, share_map)
    softmax_denominators, softmax_scaled_captions, diagonal_matched_scores = fold_texts(
        start_state, gather_rows(caption_unit_vectors, "batch"), jnp.int32(0)
    )
    encoder_output_slope = inverse_softness_factor * (
        softmax_scaled_captions / softmax_denominators[:, None] - diagonal_matched_scores
    )
    (grad_second,) = head_back(encoder_output_slope)
    grad_first_in = section_backward(grad_second, front_two, mlp_two)
    returned = hand_over(grad_first_in.astype(jnp.bfloat16))
    grad_images = section_backward(returned.astype(jnp.float32), front_one, mlp_one)
    chosen = jnp.where(phase_pick == 0, grad_images, grad_first_in)
    return chosen.transpose(1, 0, 2).reshape(count, side, side, width)[None]


def solution(mesh):
    return jax.shard_map(
        on_device,
        mesh=mesh,
        in_specs=(
            P("batch", None, None, None),
            P("phase", None, None, None),
            P("phase", None),
            P("phase", None, "mp"),
            P("phase", "mp", None),
            P(),
            P("batch", None),
            P("batch"),
        ),
        out_specs=P("phase", "batch", None, None, None),
        check_vma=False,
    )
```

```python
import jax
import jax.numpy as jnp
import numpy as np
from jax import lax
from jax.sharding import PartitionSpec as P

inverse_softness_factor = 30.0


def swapped(value, axis, stride):
    return lax.ppermute(value, axis, [(i, i ^ 1 << stride) for i in range(lax.axis_size(axis))])


def depthwise(values, kernel, side):
    margin = kernel.shape[0] // 2
    cells = side * side
    outs = []
    for o in range(cells):
        row_o, col_o = divmod(o, side)
        acc = None
        for i in range(cells):
            row_i, col_i = divmod(i, side)
            d_row, d_col = row_i - row_o, col_i - col_o
            if abs(d_row) > margin or abs(d_col) > margin:
                continue
            term = kernel[d_row + margin, d_col + margin][None, :] * values[i]
            acc = term if acc is None else acc + term
        outs.append(acc)
    return jnp.stack(outs)


def normalize_last(values):
    centred = values - jnp.mean(values, axis=-1, keepdims=True)
    variance = jnp.mean(centred * centred, axis=-1, keepdims=True)
    return centred * lax.rsqrt(variance + 1e-06)


def front_part(values, kernel, gain_vec, side):
    return normalize_last(depthwise(values, kernel, side)) * gain_vec


def mlp_part(normed, expand, project_out):
    flattened = normed.reshape(-1, normed.shape[-1]).astype(jnp.bfloat16)
    hidden = jax.nn.gelu(jnp.dot(flattened, expand, preferred_element_type=jnp.float32)).astype(
        jnp.bfloat16
    )
    return jnp.dot(hidden, project_out, preferred_element_type=jnp.float32).reshape(normed.shape)


def head_part(values, head_weight):
    pooled = jnp.mean(values, axis=0)
    normed = normalize_last(pooled).astype(jnp.bfloat16)
    embedded = jnp.dot(normed, head_weight, preferred_element_type=jnp.float32)
    return embedded * lax.rsqrt(jnp.sum(embedded * embedded, axis=-1, keepdims=True) + 1e-06)


def unit_text(texts):
    widened = texts.astype(jnp.float32)
    return (widened * lax.rsqrt(jnp.sum(widened * widened, axis=-1, keepdims=True) + 1e-06)).astype(
        jnp.bfloat16
    )


def swapped_within(value, axis, live_phase, stride):
    count = lax.axis_size(axis)
    phases = lax.axis_size("phase")
    if axis == "batch":
        pairs = [(i * phases + live_phase, (i ^ 1 << stride) * phases + live_phase) for i in range(count)]
        return lax.ppermute(value, (axis, "phase"), pairs)
    pairs = [(live_phase * count + i, live_phase * count + (i ^ 1 << stride)) for i in range(count)]
    return lax.ppermute(value, ("phase", axis), pairs)


def hidden_total(values, live_phase):
    low = values.astype(jnp.bfloat16)
    other = swapped_within(low, "mp", live_phase, 0)
    return (low.astype(jnp.float32) + other.astype(jnp.float32)).astype(jnp.bfloat16).astype(jnp.float32)


def gather_rows(block, axis, live_phase):
    count = lax.axis_size(axis)
    stride = 0
    while (1 << stride) < count:
        block = jnp.concatenate([block, swapped_within(block, axis, live_phase, stride)], axis=0)
        stride += 1
    return block


def gathered_row_ids(rows, axis):
    place = lax.axis_index(axis)
    spot = jnp.arange(rows * lax.axis_size(axis), dtype=jnp.int32)
    return jnp.bitwise_xor(place, spot // rows) * rows + spot % rows


def hand_over(values):
    return swapped(values, "phase", 0)


def section_forward(inputs_low, kernel, gain_vec, expand, project_out, side, live_phase):
    widened = inputs_low.astype(jnp.float32)
    normed, front_back = jax.vjp(lambda inner: front_part(inner, kernel, gain_vec, side), widened)
    partial_out, mlp_back = jax.vjp(lambda inner: mlp_part(inner, expand, project_out), normed)
    summed = hidden_total(partial_out, live_phase)
    return ((widened + summed).astype(jnp.bfloat16), front_back, mlp_back)


def section_backward(cotangent, front_back, mlp_back, live_phase):
    (partial_grad,) = mlp_back(cotangent)
    (from_front,) = front_back(hidden_total(partial_grad, live_phase))
    return cotangent + from_front


def make_fold(vector_lowered_total, pair_index, row_map):

    def fold_texts(state_now, text_block, first_row):
        block_rows = text_block.shape[0]
        cosine_score_matrix = inverse_softness_factor * jnp.einsum(
            "ie,je->ij", vector_lowered_total, text_block, preferred_element_type=jnp.float32
        )
        weights = jnp.exp(cosine_score_matrix).astype(jnp.bfloat16)
        softmax_denominators = jnp.sum(weights.astype(jnp.float32), axis=1)
        softmax_scaled_captions = jnp.dot(weights, text_block, preferred_element_type=jnp.float32)
        global_rows = row_map(block_rows)
        onehot = (pair_index[:, None] == global_rows[None, :]).astype(jnp.bfloat16)
        diagonal_matched_scores = jnp.dot(onehot, text_block, preferred_element_type=jnp.float32)
        return (softmax_denominators, softmax_scaled_captions, diagonal_matched_scores)

    return fold_texts


def on_device(
    images, conv_kernels, norm_gains, expand_weight, project_weight, head_weight, texts, pair_index
):
    phase_pick = lax.axis_index("phase")
    kernel = conv_kernels[0]
    gain_vec = norm_gains[0]
    expand = expand_weight[0]
    project_out = project_weight[0]
    count, side = images.shape[0], images.shape[1]
    width = images.shape[3]
    cell_major = images.reshape(count, side * side, width).transpose(1, 0, 2)
    first_out, front_one, mlp_one = section_forward(cell_major, kernel, gain_vec, expand, project_out, side, 0)
    handed = hand_over(first_out)
    second_out, front_two, mlp_two = section_forward(handed, kernel, gain_vec, expand, project_out, side, 1)
    embed, head_back = jax.vjp(
        lambda inner: head_part(inner, head_weight), second_out.astype(jnp.float32)
    )
    vector_lowered_total = embed.astype(jnp.bfloat16)
    caption_unit_vectors = unit_text(texts)
    image_rows = embed.shape[0]
    embed_width = embed.shape[1]
    text_rows = caption_unit_vectors.shape[0]
    share_count = 1
    share_rows = text_rows // share_count

    def share_map(block_rows):
        return gathered_row_ids(text_rows, "batch")

    start_state = (
        jnp.zeros((image_rows,), jnp.float32),
        jnp.zeros((image_rows, embed_width), jnp.float32),
        jnp.zeros((image_rows, embed_width), jnp.float32),
    )
    fold_texts = make_fold(vector_lowered_total, pair_index, share_map)
    softmax_denominators, softmax_scaled_captions, diagonal_matched_scores = fold_texts(
        start_state, gather_rows(caption_unit_vectors, "batch", 1), jnp.int32(0)
    )
    encoder_output_slope = inverse_softness_factor * (
        softmax_scaled_captions / softmax_denominators[:, None] - diagonal_matched_scores
    )
    (grad_second,) = head_back(encoder_output_slope)
    grad_first_in = section_backward(grad_second, front_two, mlp_two, 1)
    returned = hand_over(grad_first_in.astype(jnp.bfloat16))
    grad_images = section_backward(returned.astype(jnp.float32), front_one, mlp_one, 0)
    chosen = jnp.where(phase_pick == 0, grad_images, grad_first_in)
    return chosen.transpose(1, 0, 2).reshape(count, side, side, width)[None]


def solution(mesh):
    return jax.shard_map(
        on_device,
        mesh=mesh,
        in_specs=(
            P("batch", None, None, None),
            P("phase", None, None, None),
            P("phase", None),
            P("phase", None, "mp"),
            P("phase", "mp", None),
            P(),
            P("batch", None),
            P("batch"),
        ),
        out_specs=P("phase", "batch", None, None, None),
        check_vma=False,
    )
```

```python
import jax
import jax.numpy as jnp
import numpy as np
from jax import lax
from jax.sharding import PartitionSpec as P

inverse_softness_factor = 30.0


def swapped(value, axis, stride):
    return lax.ppermute(value, axis, [(i, i ^ 1 << stride) for i in range(lax.axis_size(axis))])


def depthwise(values, kernel, side):
    margin = kernel.shape[0] // 2
    cells = side * side
    outs = []
    for o in range(cells):
        row_o, col_o = divmod(o, side)
        acc = None
        for i in range(cells):
            row_i, col_i = divmod(i, side)
            d_row, d_col = row_i - row_o, col_i - col_o
            if abs(d_row) > margin or abs(d_col) > margin:
                continue
            term = kernel[d_row + margin, d_col + margin][None, :] * values[i]
            acc = term if acc is None else acc + term
        outs.append(acc)
    return jnp.stack(outs)


def normalize_last(values):
    centred = values - jnp.mean(values, axis=-1, keepdims=True)
    variance = jnp.mean(centred * centred, axis=-1, keepdims=True)
    return centred * lax.rsqrt(variance + 1e-06)


def front_part(values, kernel, gain_vec, side):
    return normalize_last(depthwise(values, kernel, side)) * gain_vec


def expand_part(normed, expand):
    flattened = normed.reshape(-1, normed.shape[-1]).astype(jnp.bfloat16)
    return jnp.dot(flattened, expand, preferred_element_type=jnp.float32)


def project_part(pre, project_out, shape):
    hidden = jax.nn.gelu(pre).astype(jnp.bfloat16)
    return jnp.dot(hidden, project_out, preferred_element_type=jnp.float32).reshape(shape)


def mlp_part(normed, expand, project_out):
    pre, expand_back = jax.vjp(lambda inner: expand_part(inner, expand), normed)
    branch, project_back = jax.vjp(lambda inner: project_part(inner, project_out, normed.shape), pre)

    def mlp_back(cotangent):
        (pre_grad,) = project_back(cotangent)
        return expand_back(lax.optimization_barrier(pre_grad))

    return branch, mlp_back


def head_part(values, head_weight):
    pooled = jnp.mean(values, axis=0)
    normed = normalize_last(pooled).astype(jnp.bfloat16)
    embedded = jnp.dot(normed, head_weight, preferred_element_type=jnp.float32)
    return embedded * lax.rsqrt(jnp.sum(embedded * embedded, axis=-1, keepdims=True) + 1e-06)


def unit_text(texts):
    widened = texts.astype(jnp.float32)
    return (widened * lax.rsqrt(jnp.sum(widened * widened, axis=-1, keepdims=True) + 1e-06)).astype(
        jnp.bfloat16
    )


def hidden_total(values):
    low = values.astype(jnp.bfloat16)
    other = swapped(low, "mp", 0)
    return (low.astype(jnp.float32) + other.astype(jnp.float32)).astype(jnp.bfloat16).astype(jnp.float32)


def gather_rows(block, axis):
    count = lax.axis_size(axis)
    stride = 0
    while (1 << stride) < count:
        block = jnp.concatenate([block, swapped(block, axis, stride)], axis=0)
        stride += 1
    return block


def gathered_row_ids(rows, axis):
    place = lax.axis_index(axis)
    spot = jnp.arange(rows * lax.axis_size(axis), dtype=jnp.int32)
    return jnp.bitwise_xor(place, spot // rows) * rows + spot % rows


def hand_over(values):
    return swapped(values, "phase", 0)


def section_forward(inputs_low, kernel, gain_vec, expand, project_out, side):
    widened = inputs_low.astype(jnp.float32)
    normed, front_back = jax.vjp(lambda inner: front_part(inner, kernel, gain_vec, side), widened)
    partial_out, mlp_back = mlp_part(normed, expand, project_out)
    summed = hidden_total(partial_out)
    return ((widened + summed).astype(jnp.bfloat16), front_back, mlp_back)


def section_backward(cotangent, front_back, mlp_back):
    (partial_grad,) = mlp_back(cotangent)
    (from_front,) = front_back(hidden_total(partial_grad))
    return cotangent + from_front


def make_fold(vector_lowered_total, pair_index, row_map):

    def fold_texts(state_now, text_block, first_row):
        block_rows = text_block.shape[0]
        cosine_score_matrix = inverse_softness_factor * jnp.einsum(
            "ie,je->ij", vector_lowered_total, text_block, preferred_element_type=jnp.float32
        )
        weights = jnp.exp(cosine_score_matrix).astype(jnp.bfloat16)
        softmax_denominators = jnp.sum(weights.astype(jnp.float32), axis=1)
        softmax_scaled_captions = jnp.dot(weights, text_block, preferred_element_type=jnp.float32)
        global_rows = row_map(block_rows)
        onehot = (pair_index[:, None] == global_rows[None, :]).astype(jnp.bfloat16)
        diagonal_matched_scores = jnp.dot(onehot, text_block, preferred_element_type=jnp.float32)
        return (softmax_denominators, softmax_scaled_captions, diagonal_matched_scores)

    return fold_texts


def on_device(
    images, conv_kernels, norm_gains, expand_weight, project_weight, head_weight, texts, pair_index
):
    phase_pick = lax.axis_index("phase")
    kernel = conv_kernels[0]
    gain_vec = norm_gains[0]
    expand = expand_weight[0]
    project_out = project_weight[0]
    count, side = images.shape[0], images.shape[1]
    width = images.shape[3]
    cell_major = images.reshape(count, side * side, width).transpose(1, 0, 2)
    first_out, front_one, mlp_one = section_forward(cell_major, kernel, gain_vec, expand, project_out, side)
    handed = hand_over(first_out)
    second_out, front_two, mlp_two = section_forward(handed, kernel, gain_vec, expand, project_out, side)
    embed, head_back = jax.vjp(
        lambda inner: head_part(inner, head_weight), second_out.astype(jnp.float32)
    )
    vector_lowered_total = embed.astype(jnp.bfloat16)
    caption_unit_vectors = unit_text(texts)
    image_rows = embed.shape[0]
    embed_width = embed.shape[1]
    text_rows = caption_unit_vectors.shape[0]
    share_count = 1
    share_rows = text_rows // share_count

    def share_map(block_rows):
        return gathered_row_ids(text_rows, "batch")

    start_state = (
        jnp.zeros((image_rows,), jnp.float32),
        jnp.zeros((image_rows, embed_width), jnp.float32),
        jnp.zeros((image_rows, embed_width), jnp.float32),
    )
    fold_texts = make_fold(vector_lowered_total, pair_index, share_map)
    softmax_denominators, softmax_scaled_captions, diagonal_matched_scores = fold_texts(
        start_state, gather_rows(caption_unit_vectors, "batch"), jnp.int32(0)
    )
    encoder_output_slope = inverse_softness_factor * (
        softmax_scaled_captions / softmax_denominators[:, None] - diagonal_matched_scores
    )
    (grad_second,) = head_back(encoder_output_slope)
    grad_first_in = section_backward(grad_second, front_two, mlp_two)
    returned = hand_over(grad_first_in.astype(jnp.bfloat16))
    grad_images = section_backward(returned.astype(jnp.float32), front_one, mlp_one)
    chosen = jnp.where(phase_pick == 0, grad_images, grad_first_in)
    return chosen.transpose(1, 0, 2).reshape(count, side, side, width)[None]


def solution(mesh):
    return jax.shard_map(
        on_device,
        mesh=mesh,
        in_specs=(
            P("batch", None, None, None),
            P("phase", None, None, None),
            P("phase", None),
            P("phase", None, "mp"),
            P("phase", "mp", None),
            P(),
            P("batch", None),
            P("batch"),
        ),
        out_specs=P("phase", "batch", None, None, None),
        check_vma=False,
    )
```

```python
import jax
import jax.numpy as jnp
import numpy as np
from jax import lax
from jax.sharding import PartitionSpec as P

inverse_softness_factor = 30.0


def swapped(value, axis, stride):
    return lax.ppermute(value, axis, [(i, i ^ 1 << stride) for i in range(lax.axis_size(axis))])


def depthwise(values, kernel, side):
    margin = kernel.shape[0] // 2
    cells = side * side
    outs = []
    for o in range(cells):
        row_o, col_o = divmod(o, side)
        acc = None
        for i in range(cells):
            row_i, col_i = divmod(i, side)
            d_row, d_col = row_i - row_o, col_i - col_o
            if abs(d_row) > margin or abs(d_col) > margin:
                continue
            term = kernel[d_row + margin, d_col + margin][None, :] * values[i]
            acc = term if acc is None else acc + term
        outs.append(acc)
    return jnp.stack(outs)


def normalize_last(values):
    centred = values - jnp.mean(values, axis=-1, keepdims=True)
    variance = jnp.mean(centred * centred, axis=-1, keepdims=True)
    return centred * lax.rsqrt(variance + 1e-06)


def front_part(values, kernel, gain_vec, side):
    return normalize_last(depthwise(values, kernel, side)) * gain_vec


def expand_part(normed, expand):
    flattened = normed.reshape(-1, normed.shape[-1]).astype(jnp.bfloat16)
    return jnp.dot(flattened, expand, preferred_element_type=jnp.float32)


def project_part(pre, project_out, shape):
    hidden = jax.nn.gelu(pre).astype(jnp.bfloat16)
    return jnp.dot(hidden, project_out, preferred_element_type=jnp.float32).reshape(shape)


def mlp_part(normed, expand, project_out):
    low = lax.optimization_barrier(normed.astype(jnp.bfloat16))
    pre, expand_back = jax.vjp(lambda inner: expand_part(inner, expand), low)
    branch, project_back = jax.vjp(lambda inner: project_part(inner, project_out, normed.shape), pre)

    def mlp_back(cotangent):
        (pre_grad,) = project_back(cotangent)
        (low_grad,) = expand_back(lax.optimization_barrier(pre_grad))
        return (low_grad.astype(jnp.float32),)

    return branch, mlp_back


def head_part(values, head_weight):
    pooled = jnp.mean(values, axis=0)
    normed = normalize_last(pooled).astype(jnp.bfloat16)
    embedded = jnp.dot(normed, head_weight, preferred_element_type=jnp.float32)
    return embedded * lax.rsqrt(jnp.sum(embedded * embedded, axis=-1, keepdims=True) + 1e-06)


def unit_text(texts):
    widened = texts.astype(jnp.float32)
    return (widened * lax.rsqrt(jnp.sum(widened * widened, axis=-1, keepdims=True) + 1e-06)).astype(
        jnp.bfloat16
    )


def hidden_total(values):
    low = values.astype(jnp.bfloat16)
    other = swapped(low, "mp", 0)
    return (low.astype(jnp.float32) + other.astype(jnp.float32)).astype(jnp.bfloat16).astype(jnp.float32)


def gather_rows(block, axis):
    count = lax.axis_size(axis)
    stride = 0
    while (1 << stride) < count:
        block = jnp.concatenate([block, swapped(block, axis, stride)], axis=0)
        stride += 1
    return block


def gathered_row_ids(rows, axis):
    place = lax.axis_index(axis)
    spot = jnp.arange(rows * lax.axis_size(axis), dtype=jnp.int32)
    return jnp.bitwise_xor(place, spot // rows) * rows + spot % rows


def hand_over(values):
    return swapped(values, "phase", 0)


def front_split(widened, kernel, gain_vec, side):
    conv = lax.optimization_barrier(depthwise(widened, kernel, side))
    flipped = kernel[::-1, ::-1]
    normed, norm_back = jax.vjp(lambda inner: normalize_last(inner) * gain_vec, conv)

    def front_back(cotangent):
        (conv_grad,) = norm_back(cotangent)
        return (depthwise(lax.optimization_barrier(conv_grad), flipped, side),)

    return normed, front_back


def section_forward(inputs_low, kernel, gain_vec, expand, project_out, side):
    widened = inputs_low.astype(jnp.float32)
    normed, front_back = front_split(widened, kernel, gain_vec, side)
    partial_out, mlp_back = mlp_part(normed, expand, project_out)
    summed = hidden_total(partial_out)
    return ((widened + summed).astype(jnp.bfloat16), front_back, mlp_back)


def section_backward(cotangent, front_back, mlp_back):
    (partial_grad,) = mlp_back(cotangent)
    (from_front,) = front_back(hidden_total(partial_grad))
    return cotangent + from_front


def make_fold(vector_lowered_total, pair_index, row_map):

    def fold_texts(state_now, text_block, first_row):
        block_rows = text_block.shape[0]
        cosine_score_matrix = inverse_softness_factor * jnp.einsum(
            "ie,je->ij", vector_lowered_total, text_block, preferred_element_type=jnp.float32
        )
        weights = jnp.exp(cosine_score_matrix).astype(jnp.bfloat16)
        softmax_denominators = jnp.sum(weights.astype(jnp.float32), axis=1)
        softmax_scaled_captions = jnp.dot(weights, text_block, preferred_element_type=jnp.float32)
        global_rows = row_map(block_rows)
        onehot = (pair_index[:, None] == global_rows[None, :]).astype(jnp.bfloat16)
        diagonal_matched_scores = jnp.dot(onehot, text_block, preferred_element_type=jnp.float32)
        return (softmax_denominators, softmax_scaled_captions, diagonal_matched_scores)

    return fold_texts


def on_device(
    images, conv_kernels, norm_gains, expand_weight, project_weight, head_weight, texts, pair_index
):
    phase_pick = lax.axis_index("phase")
    kernel = conv_kernels[0]
    gain_vec = norm_gains[0]
    expand = expand_weight[0]
    project_out = project_weight[0]
    count, side = images.shape[0], images.shape[1]
    width = images.shape[3]
    cell_major = images.reshape(count, side * side, width).transpose(1, 0, 2)
    first_out, front_one, mlp_one = section_forward(cell_major, kernel, gain_vec, expand, project_out, side)
    handed = hand_over(first_out)
    second_out, front_two, mlp_two = section_forward(handed, kernel, gain_vec, expand, project_out, side)
    embed, head_back = jax.vjp(
        lambda inner: head_part(inner, head_weight), second_out.astype(jnp.float32)
    )
    vector_lowered_total = embed.astype(jnp.bfloat16)
    caption_unit_vectors = unit_text(texts)
    image_rows = embed.shape[0]
    embed_width = embed.shape[1]
    text_rows = caption_unit_vectors.shape[0]
    share_count = 1
    share_rows = text_rows // share_count

    def share_map(block_rows):
        return gathered_row_ids(text_rows, "batch")

    start_state = (
        jnp.zeros((image_rows,), jnp.float32),
        jnp.zeros((image_rows, embed_width), jnp.float32),
        jnp.zeros((image_rows, embed_width), jnp.float32),
    )
    fold_texts = make_fold(vector_lowered_total, pair_index, share_map)
    softmax_denominators, softmax_scaled_captions, diagonal_matched_scores = fold_texts(
        start_state, gather_rows(caption_unit_vectors, "batch"), jnp.int32(0)
    )
    encoder_output_slope = inverse_softness_factor * (
        softmax_scaled_captions / softmax_denominators[:, None] - diagonal_matched_scores
    )
    (grad_second,) = head_back(encoder_output_slope)
    grad_first_in = section_backward(grad_second, front_two, mlp_two)
    returned = hand_over(grad_first_in.astype(jnp.bfloat16))
    grad_images = section_backward(returned.astype(jnp.float32), front_one, mlp_one)
    chosen = jnp.where(phase_pick == 0, grad_images, grad_first_in)
    return chosen.transpose(1, 0, 2).reshape(count, side, side, width)[None]


def solution(mesh):
    return jax.shard_map(
        on_device,
        mesh=mesh,
        in_specs=(
            P("batch", None, None, None),
            P("phase", None, None, None),
            P("phase", None),
            P("phase", None, "mp"),
            P("phase", "mp", None),
            P(),
            P("batch", None),
            P("batch"),
        ),
        out_specs=P("phase", "batch", None, None, None),
        check_vma=False,
    )
```

```python
import jax
import jax.numpy as jnp
import numpy as np
from jax import lax
from jax.sharding import PartitionSpec as P

inverse_softness_factor = 30.0


def swapped(value, axis, stride):
    return lax.ppermute(value, axis, [(i, i ^ 1 << stride) for i in range(lax.axis_size(axis))])


def depthwise(values, kernel, side):
    margin = kernel.shape[0] // 2
    cells = side * side
    outs = []
    for o in range(cells):
        row_o, col_o = divmod(o, side)
        acc = None
        for i in range(cells):
            row_i, col_i = divmod(i, side)
            d_row, d_col = row_i - row_o, col_i - col_o
            if abs(d_row) > margin or abs(d_col) > margin:
                continue
            term = kernel[d_row + margin, d_col + margin][None, :] * values[i]
            acc = term if acc is None else acc + term
        outs.append(acc)
    return jnp.stack(outs)


def normalize_last(values):
    centred = values - jnp.mean(values, axis=-1, keepdims=True)
    variance = jnp.mean(centred * centred, axis=-1, keepdims=True)
    return centred * lax.rsqrt(variance + 1e-06)


def front_part(values, kernel, gain_vec, side):
    return normalize_last(depthwise(values, kernel, side)) * gain_vec


def expand_part(normed, expand):
    flattened = normed.reshape(-1, normed.shape[-1]).astype(jnp.bfloat16)
    return jnp.dot(flattened, expand, preferred_element_type=jnp.float32)


def project_part(pre, project_out, shape):
    hidden = jax.nn.gelu(pre).astype(jnp.bfloat16)
    return jnp.dot(hidden, project_out, preferred_element_type=jnp.float32).reshape(shape)


def mlp_part(normed, expand, project_out):
    low = lax.optimization_barrier(normed.astype(jnp.bfloat16))
    pre, expand_back = jax.vjp(lambda inner: expand_part(inner, expand), low)
    branch, project_back = jax.vjp(lambda inner: project_part(inner, project_out, normed.shape), pre)

    def mlp_back(cotangent):
        (pre_grad,) = project_back(cotangent)
        (low_grad,) = expand_back(lax.optimization_barrier(pre_grad))
        return (low_grad.astype(jnp.float32),)

    return branch, mlp_back


def head_part(values, head_weight):
    pooled = jnp.mean(values, axis=0)
    normed = normalize_last(pooled).astype(jnp.bfloat16)
    embedded = jnp.dot(normed, head_weight, preferred_element_type=jnp.float32)
    return embedded * lax.rsqrt(jnp.sum(embedded * embedded, axis=-1, keepdims=True) + 1e-06)


def unit_text(texts):
    widened = texts.astype(jnp.float32)
    return (widened * lax.rsqrt(jnp.sum(widened * widened, axis=-1, keepdims=True) + 1e-06)).astype(
        jnp.bfloat16
    )


def hidden_total(values):
    low = values.astype(jnp.bfloat16)
    other = swapped(low, "mp", 0)
    return (low.astype(jnp.float32) + other.astype(jnp.float32)).astype(jnp.bfloat16).astype(jnp.float32)


def gather_rows(block, axis):
    count = lax.axis_size(axis)
    stride = 0
    while (1 << stride) < count:
        block = jnp.concatenate([block, swapped(block, axis, stride)], axis=0)
        stride += 1
    return block


def gathered_row_ids(rows, axis):
    place = lax.axis_index(axis)
    spot = jnp.arange(rows * lax.axis_size(axis), dtype=jnp.int32)
    return jnp.bitwise_xor(place, spot // rows) * rows + spot % rows


def hand_over(values):
    return swapped(values, "phase", 0)


def front_split(widened, kernel, gain_vec, side):
    conv = lax.optimization_barrier(depthwise(widened, kernel, side))
    flipped = kernel[::-1, ::-1]
    normed, norm_back = jax.vjp(lambda inner: normalize_last(inner) * gain_vec, conv)

    def front_back(cotangent):
        (conv_grad,) = norm_back(cotangent)
        return (depthwise(lax.optimization_barrier(conv_grad), flipped, side),)

    return normed, front_back


def section_forward(inputs_low, kernel, gain_vec, expand, project_out, side, tie=None):
    widened = inputs_low.astype(jnp.float32)
    normed, front_back = front_split(widened, kernel, gain_vec, side)
    partial_out, mlp_back = mlp_part(normed, expand, project_out)
    if tie is not None:
        partial_out = tie(partial_out)
    summed = hidden_total(partial_out)
    return ((widened + summed).astype(jnp.bfloat16), front_back, mlp_back)


def section_backward(cotangent, front_back, mlp_back):
    (partial_grad,) = mlp_back(cotangent)
    (from_front,) = front_back(hidden_total(partial_grad))
    return cotangent + from_front


def make_fold(vector_lowered_total, pair_index, row_map):

    def fold_texts(state_now, text_block, first_row):
        block_rows = text_block.shape[0]
        cosine_score_matrix = inverse_softness_factor * jnp.einsum(
            "ie,je->ij", vector_lowered_total, text_block, preferred_element_type=jnp.float32
        )
        weights = jnp.exp(cosine_score_matrix).astype(jnp.bfloat16)
        softmax_denominators = jnp.sum(weights.astype(jnp.float32), axis=1)
        softmax_scaled_captions = jnp.dot(weights, text_block, preferred_element_type=jnp.float32)
        global_rows = row_map(block_rows)
        onehot = (pair_index[:, None] == global_rows[None, :]).astype(jnp.bfloat16)
        diagonal_matched_scores = jnp.dot(onehot, text_block, preferred_element_type=jnp.float32)
        return (softmax_denominators, softmax_scaled_captions, diagonal_matched_scores)

    return fold_texts


def on_device(
    images, conv_kernels, norm_gains, expand_weight, project_weight, head_weight, texts, pair_index
):
    phase_pick = lax.axis_index("phase")
    kernel = conv_kernels[0]
    gain_vec = norm_gains[0]
    expand = expand_weight[0]
    project_out = project_weight[0]
    count, side = images.shape[0], images.shape[1]
    width = images.shape[3]
    cell_major = images.reshape(count, side * side, width).transpose(1, 0, 2)
    caption_unit_vectors = unit_text(texts)
    text_block = jnp.concatenate([caption_unit_vectors, swapped(caption_unit_vectors, "batch", 0)], axis=0)
    first_out, front_one, mlp_one = section_forward(cell_major, kernel, gain_vec, expand, project_out, side)
    first_out, text_block = lax.optimization_barrier((first_out, text_block))
    handed = hand_over(first_out)
    riding = {}

    def tie(partial_out):
        partial_out, riding["block"] = lax.optimization_barrier((partial_out, text_block))
        return partial_out

    second_out, front_two, mlp_two = section_forward(
        handed, kernel, gain_vec, expand, project_out, side, tie
    )
    all_texts = riding["block"]
    stride = 1
    while (1 << stride) < lax.axis_size("batch"):
        all_texts = jnp.concatenate([all_texts, swapped(all_texts, "batch", stride)], axis=0)
        stride += 1
    embed, head_back = jax.vjp(
        lambda inner: head_part(inner, head_weight), second_out.astype(jnp.float32)
    )
    vector_lowered_total = embed.astype(jnp.bfloat16)
    image_rows = embed.shape[0]
    embed_width = embed.shape[1]
    text_rows = caption_unit_vectors.shape[0]
    share_count = 1
    share_rows = text_rows // share_count

    def share_map(block_rows):
        return gathered_row_ids(text_rows, "batch")

    start_state = (
        jnp.zeros((image_rows,), jnp.float32),
        jnp.zeros((image_rows, embed_width), jnp.float32),
        jnp.zeros((image_rows, embed_width), jnp.float32),
    )
    fold_texts = make_fold(vector_lowered_total, pair_index, share_map)
    softmax_denominators, softmax_scaled_captions, diagonal_matched_scores = fold_texts(
        start_state, all_texts, jnp.int32(0)
    )
    encoder_output_slope = inverse_softness_factor * (
        softmax_scaled_captions / softmax_denominators[:, None] - diagonal_matched_scores
    )
    (grad_second,) = head_back(encoder_output_slope)
    grad_first_in = section_backward(grad_second, front_two, mlp_two)
    returned = hand_over(grad_first_in.astype(jnp.bfloat16))
    grad_images = section_backward(returned.astype(jnp.float32), front_one, mlp_one)
    chosen = jnp.where(phase_pick == 0, grad_images, grad_first_in)
    return chosen.transpose(1, 0, 2).reshape(count, side, side, width)[None]


def solution(mesh):
    return jax.shard_map(
        on_device,
        mesh=mesh,
        in_specs=(
            P("batch", None, None, None),
            P("phase", None, None, None),
            P("phase", None),
            P("phase", None, "mp"),
            P("phase", "mp", None),
            P(),
            P("batch", None),
            P("batch"),
        ),
        out_specs=P("phase", "batch", None, None, None),
        check_vma=False,
    )
```

```python
import jax
import jax.numpy as jnp
import numpy as np
from jax import lax
from jax.sharding import PartitionSpec as P

inverse_softness_factor = 30.0


def swapped(value, axis, stride):
    return lax.ppermute(value, axis, [(i, i ^ 1 << stride) for i in range(lax.axis_size(axis))])


def depthwise(values, kernel, side):
    margin = kernel.shape[0] // 2
    cells = side * side
    outs = []
    for o in range(cells):
        row_o, col_o = divmod(o, side)
        acc = None
        for i in range(cells):
            row_i, col_i = divmod(i, side)
            d_row, d_col = row_i - row_o, col_i - col_o
            if abs(d_row) > margin or abs(d_col) > margin:
                continue
            term = kernel[d_row + margin, d_col + margin][None, :] * values[i]
            acc = term if acc is None else acc + term
        outs.append(acc)
    return jnp.stack(outs)


def normalize_last(values):
    centred = values - jnp.mean(values, axis=-1, keepdims=True)
    variance = jnp.mean(centred * centred, axis=-1, keepdims=True)
    return centred * lax.rsqrt(variance + 1e-06)


def front_part(values, kernel, gain_vec, side):
    return normalize_last(depthwise(values, kernel, side)) * gain_vec


def expand_part(normed, expand):
    flattened = normed.reshape(-1, normed.shape[-1]).astype(jnp.bfloat16)
    return jnp.dot(flattened, expand, preferred_element_type=jnp.float32)


def project_part(pre, project_out, shape):
    hidden = jax.nn.gelu(pre).astype(jnp.bfloat16)
    return jnp.dot(hidden, project_out, preferred_element_type=jnp.float32).reshape(shape)


def mlp_part(normed, expand, project_out):
    low = lax.optimization_barrier(normed.astype(jnp.bfloat16))
    pre, expand_back = jax.vjp(lambda inner: expand_part(inner, expand), low)
    branch, project_back = jax.vjp(lambda inner: project_part(inner, project_out, normed.shape), pre)

    def mlp_back(cotangent):
        (pre_grad,) = project_back(cotangent)
        (low_grad,) = expand_back(lax.optimization_barrier(pre_grad))
        return (low_grad.astype(jnp.float32),)

    return branch, mlp_back


def head_part(values, head_weight):
    pooled = jnp.mean(values, axis=0)
    normed = normalize_last(pooled).astype(jnp.bfloat16)
    embedded = jnp.dot(normed, head_weight, preferred_element_type=jnp.float32)
    return embedded * lax.rsqrt(jnp.sum(embedded * embedded, axis=-1, keepdims=True) + 1e-06)


def unit_text(texts):
    widened = texts.astype(jnp.float32)
    return (widened * lax.rsqrt(jnp.sum(widened * widened, axis=-1, keepdims=True) + 1e-06)).astype(
        jnp.bfloat16
    )


def hidden_total(values):
    low = values.astype(jnp.bfloat16)
    other = swapped(low, "mp", 0)
    return (low.astype(jnp.float32) + other.astype(jnp.float32)).astype(jnp.bfloat16).astype(jnp.float32)


def gather_rows(block, axis):
    count = lax.axis_size(axis)
    stride = 0
    while (1 << stride) < count:
        block = jnp.concatenate([block, swapped(block, axis, stride)], axis=0)
        stride += 1
    return block


def gathered_row_ids(rows, axis):
    place = lax.axis_index(axis)
    spot = jnp.arange(rows * lax.axis_size(axis), dtype=jnp.int32)
    return jnp.bitwise_xor(place, spot // rows) * rows + spot % rows


def hand_over(values):
    return swapped(values, "phase", 0)


def front_split(widened, kernel, gain_vec, side):
    conv = lax.optimization_barrier(depthwise(widened, kernel, side))
    flipped = kernel[::-1, ::-1]
    normed, norm_back = jax.vjp(lambda inner: normalize_last(inner) * gain_vec, conv)

    def front_back(cotangent):
        (conv_grad,) = norm_back(cotangent)
        return (depthwise(lax.optimization_barrier(conv_grad), flipped, side),)

    return normed, front_back


def section_forward(inputs_low, kernel, gain_vec, expand, project_out, side, tie=None):
    widened = inputs_low.astype(jnp.float32)
    normed, front_back = front_split(widened, kernel, gain_vec, side)
    partial_out, mlp_back = mlp_part(normed, expand, project_out)
    if tie is not None:
        partial_out = tie(partial_out)
    summed = hidden_total(partial_out)
    return ((widened + summed).astype(jnp.bfloat16), front_back, mlp_back)


def section_backward(cotangent, front_back, mlp_back):
    (partial_grad,) = mlp_back(cotangent)
    (from_front,) = front_back(hidden_total(partial_grad))
    return cotangent + from_front


def make_fold(vector_lowered_total, pair_index, row_map):

    def fold_texts(state_now, text_block, first_row):
        block_rows = text_block.shape[0]
        cosine_score_matrix = inverse_softness_factor * jnp.einsum(
            "ie,je->ij", vector_lowered_total, text_block, preferred_element_type=jnp.float32
        )
        weights = jnp.exp(cosine_score_matrix).astype(jnp.bfloat16)
        softmax_denominators = jnp.sum(weights.astype(jnp.float32), axis=1)
        softmax_scaled_captions = jnp.dot(weights, text_block, preferred_element_type=jnp.float32)
        global_rows = row_map(block_rows)
        onehot = (pair_index[:, None] == global_rows[None, :]).astype(jnp.bfloat16)
        diagonal_matched_scores = jnp.dot(onehot, text_block, preferred_element_type=jnp.float32)
        return (softmax_denominators, softmax_scaled_captions, diagonal_matched_scores)

    return fold_texts


def on_device(
    images, conv_kernels, norm_gains, expand_weight, project_weight, head_weight, texts, pair_index
):
    phase_pick = lax.axis_index("phase")
    kernel = conv_kernels[0]
    gain_vec = norm_gains[0]
    expand = expand_weight[0]
    project_out = project_weight[0]
    count, side = images.shape[0], images.shape[1]
    width = images.shape[3]
    cell_major = images.reshape(count, side * side, width).transpose(1, 0, 2)
    caption_unit_vectors = unit_text(texts)
    text_block = jnp.concatenate([caption_unit_vectors, swapped(caption_unit_vectors, "batch", 0)], axis=0)
    first_out, front_one, mlp_one = section_forward(cell_major, kernel, gain_vec, expand, project_out, side)
    first_out, text_block = lax.optimization_barrier((first_out, text_block))
    handed = hand_over(first_out)
    riding = {}

    def tie(partial_out):
        partial_out, riding["block"] = lax.optimization_barrier((partial_out, text_block))
        return partial_out

    second_out, front_two, mlp_two = section_forward(
        handed, kernel, gain_vec, expand, project_out, side, tie
    )
    embed, head_back = jax.vjp(
        lambda inner: head_part(inner, head_weight), second_out.astype(jnp.float32)
    )
    all_texts = riding["block"]
    stride = 1
    while (1 << stride) < lax.axis_size("batch"):
        other = swapped(all_texts, "batch", stride)
        stride += 1
        if (1 << stride) >= lax.axis_size("batch"):
            embed, other = lax.optimization_barrier((embed, other))
        all_texts = jnp.concatenate([all_texts, other], axis=0)
    vector_lowered_total = embed.astype(jnp.bfloat16)
    image_rows = embed.shape[0]
    embed_width = embed.shape[1]
    text_rows = caption_unit_vectors.shape[0]
    share_count = 1
    share_rows = text_rows // share_count

    def share_map(block_rows):
        return gathered_row_ids(text_rows, "batch")

    start_state = (
        jnp.zeros((image_rows,), jnp.float32),
        jnp.zeros((image_rows, embed_width), jnp.float32),
        jnp.zeros((image_rows, embed_width), jnp.float32),
    )
    fold_texts = make_fold(vector_lowered_total, pair_index, share_map)
    softmax_denominators, softmax_scaled_captions, diagonal_matched_scores = fold_texts(
        start_state, all_texts, jnp.int32(0)
    )
    encoder_output_slope = inverse_softness_factor * (
        softmax_scaled_captions / softmax_denominators[:, None] - diagonal_matched_scores
    )
    (grad_second,) = head_back(encoder_output_slope)
    grad_first_in = section_backward(grad_second, front_two, mlp_two)
    returned = hand_over(grad_first_in.astype(jnp.bfloat16))
    grad_images = section_backward(returned.astype(jnp.float32), front_one, mlp_one)
    chosen = jnp.where(phase_pick == 0, grad_images, grad_first_in)
    return chosen.transpose(1, 0, 2).reshape(count, side, side, width)[None]


def solution(mesh):
    return jax.shard_map(
        on_device,
        mesh=mesh,
        in_specs=(
            P("batch", None, None, None),
            P("phase", None, None, None),
            P("phase", None),
            P("phase", None, "mp"),
            P("phase", "mp", None),
            P(),
            P("batch", None),
            P("batch"),
        ),
        out_specs=P("phase", "batch", None, None, None),
        check_vma=False,
    )
```

```python
import jax
import jax.numpy as jnp
import numpy as np
from jax import lax
from jax.sharding import PartitionSpec as P

inverse_softness_factor = 30.0


def swapped(value, axis, stride):
    return lax.ppermute(value, axis, [(i, i ^ 1 << stride) for i in range(lax.axis_size(axis))])


def depthwise(values, kernel, side):
    margin = kernel.shape[0] // 2
    cells = side * side
    outs = []
    for o in range(cells):
        row_o, col_o = divmod(o, side)
        acc = None
        for i in range(cells):
            row_i, col_i = divmod(i, side)
            d_row, d_col = row_i - row_o, col_i - col_o
            if abs(d_row) > margin or abs(d_col) > margin:
                continue
            term = kernel[d_row + margin, d_col + margin][None, :] * values[i]
            acc = term if acc is None else acc + term
        outs.append(acc)
    return jnp.stack(outs)


def normalize_last(values):
    centred = values - jnp.mean(values, axis=-1, keepdims=True)
    variance = jnp.mean(centred * centred, axis=-1, keepdims=True)
    return centred * lax.rsqrt(variance + 1e-06)


def front_part(values, kernel, gain_vec, side):
    return normalize_last(depthwise(values, kernel, side)) * gain_vec


def expand_part(normed, expand):
    flattened = normed.reshape(-1, normed.shape[-1]).astype(jnp.bfloat16)
    return jnp.dot(flattened, expand, preferred_element_type=jnp.float32)


def project_part(pre, project_out, shape):
    hidden = jax.nn.gelu(pre).astype(jnp.bfloat16)
    return jnp.dot(hidden, project_out, preferred_element_type=jnp.float32).reshape(shape)


def mlp_part(normed, expand, project_out):
    low = lax.optimization_barrier(normed.astype(jnp.bfloat16))
    pre, expand_back = jax.vjp(lambda inner: expand_part(inner, expand), low)
    hidden = jax.nn.gelu(pre).astype(jnp.bfloat16)
    branch, hidden_back = jax.vjp(
        lambda inner: jnp.dot(inner, project_out, preferred_element_type=jnp.float32).reshape(normed.shape),
        hidden,
    )
    slope = lax.optimization_barrier(jax.jvp(jax.nn.gelu, (pre,), (jnp.ones_like(pre),))[1])

    def mlp_back(cotangent):
        (hidden_grad,) = hidden_back(cotangent)
        pre_grad = hidden_grad.astype(jnp.float32) * slope
        (low_grad,) = expand_back(lax.optimization_barrier(pre_grad))
        return (low_grad.astype(jnp.float32),)

    return branch, mlp_back


def head_part(values, head_weight):
    pooled = jnp.mean(values, axis=0)
    normed = normalize_last(pooled).astype(jnp.bfloat16)
    embedded = jnp.dot(normed, head_weight, preferred_element_type=jnp.float32)
    return embedded * lax.rsqrt(jnp.sum(embedded * embedded, axis=-1, keepdims=True) + 1e-06)


def unit_text(texts):
    widened = texts.astype(jnp.float32)
    return (widened * lax.rsqrt(jnp.sum(widened * widened, axis=-1, keepdims=True) + 1e-06)).astype(
        jnp.bfloat16
    )


def hidden_total(values):
    low = values.astype(jnp.bfloat16)
    other = swapped(low, "mp", 0)
    return (low.astype(jnp.float32) + other.astype(jnp.float32)).astype(jnp.bfloat16).astype(jnp.float32)


def gather_rows(block, axis):
    count = lax.axis_size(axis)
    stride = 0
    while (1 << stride) < count:
        block = jnp.concatenate([block, swapped(block, axis, stride)], axis=0)
        stride += 1
    return block


def gathered_row_ids(rows, axis):
    place = lax.axis_index(axis)
    spot = jnp.arange(rows * lax.axis_size(axis), dtype=jnp.int32)
    return jnp.bitwise_xor(place, spot // rows) * rows + spot % rows


def hand_over(values):
    return swapped(values, "phase", 0)


def front_split(widened, kernel, gain_vec, side):
    conv = lax.optimization_barrier(depthwise(widened, kernel, side))
    flipped = kernel[::-1, ::-1]
    normed, norm_back = jax.vjp(lambda inner: normalize_last(inner) * gain_vec, conv)

    def front_back(cotangent):
        (conv_grad,) = norm_back(cotangent)
        return (depthwise(lax.optimization_barrier(conv_grad), flipped, side),)

    return normed, front_back


def section_forward(inputs_low, kernel, gain_vec, expand, project_out, side, tie=None):
    widened = inputs_low.astype(jnp.float32)
    normed, front_back = front_split(widened, kernel, gain_vec, side)
    partial_out, mlp_back = mlp_part(normed, expand, project_out)
    if tie is not None:
        partial_out = tie(partial_out)
    summed = hidden_total(partial_out)
    return ((widened + summed).astype(jnp.bfloat16), front_back, mlp_back)


def section_backward(cotangent, front_back, mlp_back):
    (partial_grad,) = mlp_back(cotangent)
    (from_front,) = front_back(hidden_total(partial_grad))
    return cotangent + from_front


def make_fold(vector_lowered_total, pair_index, row_map):

    def fold_texts(state_now, text_block, first_row):
        block_rows = text_block.shape[0]
        cosine_score_matrix = inverse_softness_factor * jnp.einsum(
            "ie,je->ij", vector_lowered_total, text_block, preferred_element_type=jnp.float32
        )
        weights = jnp.exp(cosine_score_matrix).astype(jnp.bfloat16)
        softmax_denominators = jnp.sum(weights.astype(jnp.float32), axis=1)
        softmax_scaled_captions = jnp.dot(weights, text_block, preferred_element_type=jnp.float32)
        global_rows = row_map(block_rows)
        onehot = (pair_index[:, None] == global_rows[None, :]).astype(jnp.bfloat16)
        diagonal_matched_scores = jnp.dot(onehot, text_block, preferred_element_type=jnp.float32)
        return (softmax_denominators, softmax_scaled_captions, diagonal_matched_scores)

    return fold_texts


def on_device(
    images, conv_kernels, norm_gains, expand_weight, project_weight, head_weight, texts, pair_index
):
    phase_pick = lax.axis_index("phase")
    kernel = conv_kernels[0]
    gain_vec = norm_gains[0]
    expand = expand_weight[0]
    project_out = project_weight[0]
    count, side = images.shape[0], images.shape[1]
    width = images.shape[3]
    cell_major = images.reshape(count, side * side, width).transpose(1, 0, 2)
    caption_unit_vectors = unit_text(texts)
    text_block = jnp.concatenate([caption_unit_vectors, swapped(caption_unit_vectors, "batch", 0)], axis=0)
    first_out, front_one, mlp_one = section_forward(cell_major, kernel, gain_vec, expand, project_out, side)
    first_out, text_block = lax.optimization_barrier((first_out, text_block))
    handed = hand_over(first_out)
    riding = {}

    def tie(partial_out):
        partial_out, riding["block"] = lax.optimization_barrier((partial_out, text_block))
        return partial_out

    second_out, front_two, mlp_two = section_forward(
        handed, kernel, gain_vec, expand, project_out, side, tie
    )
    embed, head_back = jax.vjp(
        lambda inner: head_part(inner, head_weight), second_out.astype(jnp.float32)
    )
    all_texts = riding["block"]
    stride = 1
    while (1 << stride) < lax.axis_size("batch"):
        other = swapped(all_texts, "batch", stride)
        stride += 1
        if (1 << stride) >= lax.axis_size("batch"):
            embed, other = lax.optimization_barrier((embed, other))
        all_texts = jnp.concatenate([all_texts, other], axis=0)
    vector_lowered_total = embed.astype(jnp.bfloat16)
    image_rows = embed.shape[0]
    embed_width = embed.shape[1]
    text_rows = caption_unit_vectors.shape[0]
    share_count = 1
    share_rows = text_rows // share_count

    def share_map(block_rows):
        return gathered_row_ids(text_rows, "batch")

    start_state = (
        jnp.zeros((image_rows,), jnp.float32),
        jnp.zeros((image_rows, embed_width), jnp.float32),
        jnp.zeros((image_rows, embed_width), jnp.float32),
    )
    fold_texts = make_fold(vector_lowered_total, pair_index, share_map)
    softmax_denominators, softmax_scaled_captions, diagonal_matched_scores = fold_texts(
        start_state, all_texts, jnp.int32(0)
    )
    encoder_output_slope = inverse_softness_factor * (
        softmax_scaled_captions / softmax_denominators[:, None] - diagonal_matched_scores
    )
    (grad_second,) = head_back(encoder_output_slope)
    grad_first_in = section_backward(grad_second, front_two, mlp_two)
    returned = hand_over(grad_first_in.astype(jnp.bfloat16))
    grad_images = section_backward(returned.astype(jnp.float32), front_one, mlp_one)
    chosen = jnp.where(phase_pick == 0, grad_images, grad_first_in)
    return chosen.transpose(1, 0, 2).reshape(count, side, side, width)[None]


def solution(mesh):
    return jax.shard_map(
        on_device,
        mesh=mesh,
        in_specs=(
            P("batch", None, None, None),
            P("phase", None, None, None),
            P("phase", None),
            P("phase", None, "mp"),
            P("phase", "mp", None),
            P(),
            P("batch", None),
            P("batch"),
        ),
        out_specs=P("phase", "batch", None, None, None),
        check_vma=False,
    )
```

```python
import jax
import jax.numpy as jnp
import numpy as np
from jax import lax
from jax.sharding import PartitionSpec as P

inverse_softness_factor = 30.0


def swapped(value, axis, stride):
    return lax.ppermute(value, axis, [(i, i ^ 1 << stride) for i in range(lax.axis_size(axis))])


def depthwise(values, kernel, side):
    margin = kernel.shape[0] // 2
    cells = side * side
    outs = []
    for o in range(cells):
        row_o, col_o = divmod(o, side)
        acc = None
        for i in range(cells):
            row_i, col_i = divmod(i, side)
            d_row, d_col = row_i - row_o, col_i - col_o
            if abs(d_row) > margin or abs(d_col) > margin:
                continue
            term = kernel[d_row + margin, d_col + margin][None, :] * values[i]
            acc = term if acc is None else acc + term
        outs.append(acc)
    return jnp.stack(outs)


def normalize_last(values):
    centred = values - jnp.mean(values, axis=-1, keepdims=True)
    variance = jnp.mean(centred * centred, axis=-1, keepdims=True)
    return centred * lax.rsqrt(variance + 1e-06)


def front_part(values, kernel, gain_vec, side):
    return normalize_last(depthwise(values, kernel, side)) * gain_vec


def expand_part(normed, expand):
    flattened = normed.reshape(-1, normed.shape[-1]).astype(jnp.bfloat16)
    return jnp.dot(flattened, expand, preferred_element_type=jnp.float32)


def project_part(pre, project_out, shape):
    hidden = jax.nn.gelu(pre).astype(jnp.bfloat16)
    return jnp.dot(hidden, project_out, preferred_element_type=jnp.float32).reshape(shape)


def mlp_part(normed, expand, project_out):
    low = lax.optimization_barrier(normed.astype(jnp.bfloat16))
    pre, expand_back = jax.vjp(lambda inner: expand_part(inner, expand), low)
    hidden = jax.nn.gelu(pre).astype(jnp.bfloat16)
    branch, hidden_back = jax.vjp(
        lambda inner: jnp.dot(inner, project_out, preferred_element_type=jnp.float32).reshape(normed.shape),
        hidden,
    )
    slope = lax.optimization_barrier(jax.jvp(jax.nn.gelu, (pre,), (jnp.ones_like(pre),))[1])

    def mlp_back(cotangent):
        (hidden_grad,) = hidden_back(cotangent)
        pre_grad = hidden_grad.astype(jnp.float32) * slope
        low_pre_grad = lax.optimization_barrier(pre_grad.astype(jnp.bfloat16))
        (low_grad,) = expand_back(low_pre_grad.astype(jnp.float32))
        return (low_grad.astype(jnp.float32),)

    return branch, mlp_back


def head_part(values, head_weight):
    pooled = jnp.mean(values, axis=0)
    normed = normalize_last(pooled).astype(jnp.bfloat16)
    embedded = jnp.dot(normed, head_weight, preferred_element_type=jnp.float32)
    return embedded * lax.rsqrt(jnp.sum(embedded * embedded, axis=-1, keepdims=True) + 1e-06)


def unit_text(texts):
    widened = texts.astype(jnp.float32)
    return (widened * lax.rsqrt(jnp.sum(widened * widened, axis=-1, keepdims=True) + 1e-06)).astype(
        jnp.bfloat16
    )


def hidden_total(values):
    low = values.astype(jnp.bfloat16)
    other = swapped(low, "mp", 0)
    return (low.astype(jnp.float32) + other.astype(jnp.float32)).astype(jnp.bfloat16).astype(jnp.float32)


def gather_rows(block, axis):
    count = lax.axis_size(axis)
    stride = 0
    while (1 << stride) < count:
        block = jnp.concatenate([block, swapped(block, axis, stride)], axis=0)
        stride += 1
    return block


def gathered_row_ids(rows, axis):
    place = lax.axis_index(axis)
    spot = jnp.arange(rows * lax.axis_size(axis), dtype=jnp.int32)
    return jnp.bitwise_xor(place, spot // rows) * rows + spot % rows


def hand_over(values):
    return swapped(values, "phase", 0)


def front_split(widened, kernel, gain_vec, side):
    conv = lax.optimization_barrier(depthwise(widened, kernel, side))
    flipped = kernel[::-1, ::-1]
    normed, norm_back = jax.vjp(lambda inner: normalize_last(inner) * gain_vec, conv)

    def front_back(cotangent):
        (conv_grad,) = norm_back(cotangent)
        return (depthwise(lax.optimization_barrier(conv_grad), flipped, side),)

    return normed, front_back


def section_forward(inputs_low, kernel, gain_vec, expand, project_out, side, tie=None):
    widened = inputs_low.astype(jnp.float32)
    normed, front_back = front_split(widened, kernel, gain_vec, side)
    partial_out, mlp_back = mlp_part(normed, expand, project_out)
    if tie is not None:
        partial_out = tie(partial_out)
    summed = hidden_total(partial_out)
    return ((widened + summed).astype(jnp.bfloat16), front_back, mlp_back)


def section_backward(cotangent, front_back, mlp_back):
    (partial_grad,) = mlp_back(cotangent)
    (from_front,) = front_back(hidden_total(partial_grad))
    return cotangent + from_front


def make_fold(vector_lowered_total, pair_index, row_map):

    def fold_texts(state_now, text_block, first_row):
        block_rows = text_block.shape[0]
        cosine_score_matrix = inverse_softness_factor * jnp.einsum(
            "ie,je->ij", vector_lowered_total, text_block, preferred_element_type=jnp.float32
        )
        weights = jnp.exp(cosine_score_matrix).astype(jnp.bfloat16)
        softmax_denominators = jnp.sum(weights.astype(jnp.float32), axis=1)
        softmax_scaled_captions = jnp.dot(weights, text_block, preferred_element_type=jnp.float32)
        global_rows = row_map(block_rows)
        onehot = (pair_index[:, None] == global_rows[None, :]).astype(jnp.bfloat16)
        diagonal_matched_scores = jnp.dot(onehot, text_block, preferred_element_type=jnp.float32)
        return (softmax_denominators, softmax_scaled_captions, diagonal_matched_scores)

    return fold_texts


def on_device(
    images, conv_kernels, norm_gains, expand_weight, project_weight, head_weight, texts, pair_index
):
    phase_pick = lax.axis_index("phase")
    kernel = conv_kernels[0]
    gain_vec = norm_gains[0]
    expand = expand_weight[0]
    project_out = project_weight[0]
    count, side = images.shape[0], images.shape[1]
    width = images.shape[3]
    cell_major = images.reshape(count, side * side, width).transpose(1, 0, 2)
    caption_unit_vectors = unit_text(texts)
    text_block = jnp.concatenate([caption_unit_vectors, swapped(caption_unit_vectors, "batch", 0)], axis=0)
    first_out, front_one, mlp_one = section_forward(cell_major, kernel, gain_vec, expand, project_out, side)
    first_out, text_block = lax.optimization_barrier((first_out, text_block))
    handed = hand_over(first_out)
    riding = {}

    def tie(partial_out):
        partial_out, riding["block"] = lax.optimization_barrier((partial_out, text_block))
        return partial_out

    second_out, front_two, mlp_two = section_forward(
        handed, kernel, gain_vec, expand, project_out, side, tie
    )
    embed, head_back = jax.vjp(
        lambda inner: head_part(inner, head_weight), second_out.astype(jnp.float32)
    )
    all_texts = riding["block"]
    stride = 1
    while (1 << stride) < lax.axis_size("batch"):
        other = swapped(all_texts, "batch", stride)
        stride += 1
        if (1 << stride) >= lax.axis_size("batch"):
            embed, other = lax.optimization_barrier((embed, other))
        all_texts = jnp.concatenate([all_texts, other], axis=0)
    vector_lowered_total = embed.astype(jnp.bfloat16)
    image_rows = embed.shape[0]
    embed_width = embed.shape[1]
    text_rows = caption_unit_vectors.shape[0]
    share_count = 1
    share_rows = text_rows // share_count

    def share_map(block_rows):
        return gathered_row_ids(text_rows, "batch")

    start_state = (
        jnp.zeros((image_rows,), jnp.float32),
        jnp.zeros((image_rows, embed_width), jnp.float32),
        jnp.zeros((image_rows, embed_width), jnp.float32),
    )
    fold_texts = make_fold(vector_lowered_total, pair_index, share_map)
    softmax_denominators, softmax_scaled_captions, diagonal_matched_scores = fold_texts(
        start_state, all_texts, jnp.int32(0)
    )
    encoder_output_slope = inverse_softness_factor * (
        softmax_scaled_captions / softmax_denominators[:, None] - diagonal_matched_scores
    )
    (grad_second,) = head_back(encoder_output_slope)
    grad_first_in = section_backward(grad_second, front_two, mlp_two)
    returned = hand_over(grad_first_in.astype(jnp.bfloat16))
    grad_images = section_backward(returned.astype(jnp.float32), front_one, mlp_one)
    chosen = jnp.where(phase_pick == 0, grad_images, grad_first_in)
    return chosen.transpose(1, 0, 2).reshape(count, side, side, width)[None]


def solution(mesh):
    return jax.shard_map(
        on_device,
        mesh=mesh,
        in_specs=(
            P("batch", None, None, None),
            P("phase", None, None, None),
            P("phase", None),
            P("phase", None, "mp"),
            P("phase", "mp", None),
            P(),
            P("batch", None),
            P("batch"),
        ),
        out_specs=P("phase", "batch", None, None, None),
        check_vma=False,
    )
```
